256 devices in a mesh: section: 16 (over y, x_hi, core), expert: 16 (over x_lo, z).
Axes of the slice: x: 4 (x_hi: 2, x_lo: 2; x = x_hi * 2 + x_lo), y: 4, z: 8, core: 2. Of those that a mesh axis runs over, the one named last changes fastest.
Arguments:
- tokens: bfloat16 [16, 2048, 7168], P('section', 'expert'), may hold values from -6 to 6
- cotangent: bfloat16 [16, 2048, 7168], P('section', 'expert'), may hold values from -6 to 6
- expert_ids: int32 [16, 2048, 8], P('section', 'expert'), may hold values from 0 to 31, as said below
- slot_index: int32 [16, 2048, 8], P('section', 'expert'), may hold values from 0 to 31, as said below
- gate_scale: float32 [16, 2048, 8], P('section', 'expert'), may hold values from 0.2 to 1.2
- gate_weight: bfloat16 [16, 7168, 2048], P('section', None, 'expert'), may hold values from -0.0625 to 0.0625
- up_weight: bfloat16 [16, 7168, 2048], P('section', None, 'expert'), may hold values from -0.0625 to 0.0625
- down_weight: bfloat16 [16, 2048, 7168], P('section', 'expert'), may hold values from -0.125 to 0.125
Outputs:
- next_input: bfloat16 [16, 2048, 7168], P('section', 'expert')
- prior_grad: bfloat16 [16, 2048, 7168], P('section', 'expert')
The draws below stay inside these ranges and needn't reach their ends.
Inputs may be any that keep to these rules, and one draw needn't show every extreme that they name: `expert_ids`: each token names 8 different experts; among the 128 tokens of one device every expert is named exactly 32 times. `slot_index`: among the routes of one device's tokens to one expert, the slots are 0 to 31, each once.
All inputs are finite; a program needn't handle non-finite values.
Results may differ from the reference program's by a relative error of at most 0.011.
Values may be sent and summed in bfloat16 or wider, within the bound.
No kernel may reach another device: no remote copies, remote signals or barrier semaphores. Data moves between devices by JAX's collectives and lax.ppermute only.
A program may use at most 128 MiB of HBM per device.

```python
import jax
import jax.numpy as jnp
from jax import lax

D = 7168
HID = 2048
EXPERTS = 32
TOP = 8
TOK_DEV = 128
LAYERS = 16
TOKENS = 2048
CAP = 32
N_EXPERT = 16


def routing_tables(key):
    blocks = LAYERS * TOKENS // TOK_DEV
    groups = TOK_DEV // EXPERTS

    def one_block(block_key):
        first, second, third, fourth = jax.random.split(block_key, 4)
        offset_keys = jax.random.split(first, groups)
        offsets = jax.vmap(lambda kk: jax.random.permutation(kk, EXPERTS)[:TOP])(offset_keys).astype(jnp.int32)
        within = jnp.arange(EXPERTS, dtype=jnp.int32)
        raw = (offsets[:, None, :] + within[None, :, None]) % EXPERTS
        raw = raw.reshape(TOK_DEV, TOP)
        relabel = jax.random.permutation(second, EXPERTS).astype(jnp.int32)
        order = jax.random.permutation(third, TOK_DEV).astype(jnp.int32)
        named = relabel[raw][order]
        score = jax.random.permutation(fourth, TOK_DEV * TOP).astype(jnp.int32)
        flat_named = named.reshape(-1)
        same = flat_named[:, None] == flat_named[None, :]
        lower = score[None, :] < score[:, None]
        slots = jnp.sum((same & lower).astype(jnp.int32), axis=1).reshape(TOK_DEV, TOP)
        return (named.astype(jnp.int32), slots.astype(jnp.int32))
    keys = jax.random.split(key, blocks)
    named, slots = lax.map(one_block, keys)
    return (named.reshape(LAYERS, TOKENS, TOP), slots.reshape(LAYERS, TOKENS, TOP))


def draw_expert_ids(key, part):
    return routing_tables(jax.random.fold_in(key, 7))[0]


def draw_slot_index(key, part):
    return routing_tables(jax.random.fold_in(key, 7))[1]


def levels(own_key, extent, cuts, least, top_value):
    def one(dim, shards_of):
        steps = jax.random.uniform(jax.random.fold_in(jax.random.fold_in(own_key, 6), dim), (shards_of,), jnp.float32, least / len(cuts), top_value / len(cuts))
        return jnp.repeat(jnp.exp(steps), extent[dim] // shards_of).reshape((-1,) + (1,) * (len(extent) - dim - 1))

    factor_of = one(*cuts[0])
    for cut in cuts[1:]:
        factor_of = factor_of * one(*cut)
    return factor_of


def scatter_about(rng, dims, spread, bound, shards=(), kind=jnp.bfloat16):
    result = spread * jax.random.normal(rng, dims, jnp.float32)
    if shards:
        result = result * levels(rng, dims, shards, -0.22, 0.18)
    return jnp.clip(result, -bound, bound).astype(kind)


def setup_inputs(seed: int = 0) -> dict:
    splits = jax.random.split(jax.random.key(seed), 9)
    tokens = scatter_about(splits[0], (LAYERS, TOKENS, D), 1.0, 6.0, ((0, 16), (1, 16)))
    cotangent = scatter_about(splits[1], (LAYERS, TOKENS, D), 1.0, 6.0, ((0, 16), (1, 16)))
    expert_ids = draw_expert_ids(jax.random.fold_in(splits[8], 71), 0)
    slot_index = draw_slot_index(jax.random.fold_in(splits[8], 71), 0)
    gate_scale = jnp.clip(0.2 + 1 * jax.random.uniform(splits[4], (LAYERS, TOKENS, TOP), jnp.float32) ** levels(splits[4], (LAYERS, TOKENS, TOP), ((0, 16), (1, 16)), -0.2, 0.2), 0.2, 1.2)
    gate_weight = scatter_about(splits[5], (LAYERS, D, HID), D ** -0.5, 0.0625, ((0, 16), (2, 16)))
    up_weight = scatter_about(splits[6], (LAYERS, D, HID), D ** -0.5, 0.0625, ((0, 16), (2, 16)))
    down_weight = scatter_about(splits[7], (LAYERS, HID, D), HID ** -0.5, 0.125, ((0, 16), (1, 16)))
    return dict(tokens=tokens, cotangent=cotangent, expert_ids=expert_ids, slot_index=slot_index, gate_scale=gate_scale, gate_weight=gate_weight, up_weight=up_weight, down_weight=down_weight)


def silu_parts(gate):
    sig = jax.nn.sigmoid(gate)
    return gate * sig, sig * (1.0 + gate * (1.0 - sig))


def rounded(value):
    return lax.optimization_barrier(value.astype(jnp.bfloat16)).astype(jnp.float32)


def one_section(section, tokens, cotangent, ids, slots, scale, gate_w, up_w, down_w):
    rows_all = CAP * N_EXPERT
    hit = ids == section
    chosen = jnp.any(hit, axis=1)
    slot = jnp.sum(jnp.where(hit, slots, 0), axis=1).astype(jnp.int32)
    weight = jnp.sum(jnp.where(hit, scale, jnp.float32(0.0)), axis=1)
    block = jnp.arange(tokens.shape[0], dtype=jnp.int32) // TOK_DEV
    place = (block * CAP + slot).astype(jnp.int32)
    dest = jnp.where(chosen, place, rows_all).astype(jnp.int32)
    sent = jnp.zeros((rows_all, D), jnp.bfloat16).at[dest].set(tokens, mode="drop")
    carried = (weight[:, None] * cotangent.astype(jnp.float32)).astype(jnp.bfloat16)
    back = jnp.zeros((rows_all, D), jnp.bfloat16).at[dest].set(carried, mode="drop")
    gate = jnp.dot(sent, gate_w, preferred_element_type=jnp.float32)
    up = jnp.dot(sent, up_w, preferred_element_type=jnp.float32)
    act, slope = silu_parts(gate)
    hidden = (act * up).astype(jnp.bfloat16)
    grad_hidden = jnp.dot(back, down_w.T, preferred_element_type=jnp.float32)
    grad_up = (grad_hidden * act).astype(jnp.bfloat16)
    grad_gate = (grad_hidden * up * slope).astype(jnp.bfloat16)
    width = HID // N_EXPERT

    def add_share(carry, index):
        start = (index * width).astype(jnp.int32)
        hid_part = lax.dynamic_slice_in_dim(hidden, start, width, 1)
        down_part = lax.dynamic_slice_in_dim(down_w, start, width, 0)
        gate_part = lax.dynamic_slice_in_dim(gate_w, start, width, 1)
        up_part = lax.dynamic_slice_in_dim(up_w, start, width, 1)
        gg_part = lax.dynamic_slice_in_dim(grad_gate, start, width, 1)
        gu_part = lax.dynamic_slice_in_dim(grad_up, start, width, 1)
        ahead = jnp.dot(hid_part, down_part, preferred_element_type=jnp.float32)
        behind = jnp.dot(gg_part, gate_part.T, preferred_element_type=jnp.float32)
        behind = behind + jnp.dot(gu_part, up_part.T, preferred_element_type=jnp.float32)
        return (carry[0] + rounded(ahead), carry[1] + rounded(behind)), None

    zeros = jnp.zeros((rows_all, D), jnp.float32)
    (combined, inward), _ = lax.scan(add_share, (zeros, zeros), jnp.arange(N_EXPERT, dtype=jnp.int32))
    output = tokens.astype(jnp.float32) + weight[:, None] * combined[place]
    grad_in = cotangent.astype(jnp.float32) + jnp.where(chosen[:, None], inward[place], jnp.float32(0.0))
    return output.astype(jnp.bfloat16), grad_in.astype(jnp.bfloat16)


def reference(tokens, cotangent, expert_ids, slot_index, gate_scale, gate_weight, up_weight, down_weight):
    ahead_list = []
    behind_list = []
    for section in range(LAYERS):
        output, grad_in = one_section(section, tokens[section], cotangent[section], expert_ids[section], slot_index[section], gate_scale[section], gate_weight[section], up_weight[section], down_weight[section])
        ahead_list.append(output)
        behind_list.append(grad_in)
    ahead = jnp.stack(ahead_list)
    behind = jnp.stack(behind_list)
    next_input = jnp.concatenate([jnp.zeros_like(ahead[:1]), ahead[:-1]], axis=0)
    prior_grad = jnp.concatenate([behind[1:], jnp.zeros_like(behind[:1])], axis=0)
    return next_input, prior_grad
```

```python
import jax
import jax.numpy as jnp
from jax import lax
from jax.sharding import PartitionSpec as P

CAP = 32


def from_behind(x, axis, by):
    length = lax.axis_size(axis)
    pairs = [(i, i + by) for i in range(length) if 0 <= i + by < length]
    return lax.ppermute(x, axis, pairs)


def silu_parts(gate):
    sig = jax.nn.sigmoid(gate)
    return (gate * sig, sig * (1.0 + gate * (1.0 - sig)))


def pick_rows(route, rows, bulk):
    taken = jnp.take(rows, jnp.maximum(route - 1, 0), axis=0)
    return jnp.where((route > 0)[:, None], taken, bulk)


def body(
    tokens, cotangent, expert_ids, slot_index, gate_scale, gate_weight, up_weight, down_weight
):
    section = lax.axis_index("section")
    local = tokens[0]
    grad_out = cotangent[0]
    named = expert_ids[0]
    gate_mat = gate_weight[0]
    up_mat = up_weight[0]
    down_mat = down_weight[0]
    width_local = gate_mat.shape[1]
    hit = named == section
    chosen = jnp.any(hit, axis=1)
    slot = jnp.sum(jnp.where(hit, slot_index[0], 0), axis=1)
    weight = jnp.sum(jnp.where(hit, gate_scale[0], jnp.float32(0.0)), axis=1)
    route = jnp.where(chosen, slot + 1, 0).astype(jnp.int32)

    tok_prev = from_behind(local, "section", 1)
    cot_next = from_behind(grad_out, "section", -1)
    route_prev = from_behind(route, "section", 1)
    route_next = from_behind(route, "section", -1)

    places = jnp.arange(CAP, dtype=jnp.int32)
    mask = (places[:, None] == slot[None, :]) & chosen[None, :]
    table = mask.astype(jnp.bfloat16)
    sent = jnp.dot(table, local, preferred_element_type=jnp.float32).astype(jnp.bfloat16)
    cot_sent = jnp.dot(table, grad_out, preferred_element_type=jnp.float32).astype(jnp.bfloat16)
    wslot = jnp.sum(jnp.where(mask, weight[None, :], jnp.float32(0.0)), axis=1)
    back = (wslot[:, None] * cot_sent.astype(jnp.float32)).astype(jnp.bfloat16)
    piece = lax.all_gather(sent, "expert", axis=0, tiled=True)
    gate_up = jnp.concatenate(
        [
            jnp.dot(piece, gate_mat, preferred_element_type=jnp.float32),
            jnp.dot(piece, up_mat, preferred_element_type=jnp.float32),
        ],
        axis=1,
    )
    gate = gate_up[:, :width_local]
    up = gate_up[:, width_local:]
    act, slope = silu_parts(gate)
    hidden = (act * up).astype(jnp.bfloat16)
    combined = lax.psum_scatter(
        jnp.dot(hidden, down_mat, preferred_element_type=jnp.float32).astype(jnp.bfloat16),
        "expert",
        scatter_dimension=0,
        tiled=True,
    ).astype(jnp.float32)
    grad_hidden = jnp.dot(
        lax.all_gather(back, "expert", axis=0, tiled=True),
        down_mat.T,
        preferred_element_type=jnp.float32,
    )
    grad_up = (grad_hidden * act).astype(jnp.bfloat16)
    grad_gate = (grad_hidden * up * slope).astype(jnp.bfloat16)
    behind = jnp.dot(grad_gate, gate_mat.T, preferred_element_type=jnp.float32)
    inward = lax.psum_scatter(
        (behind + jnp.dot(grad_up, up_mat.T, preferred_element_type=jnp.float32)).astype(
            jnp.bfloat16
        ),
        "expert",
        scatter_dimension=0,
        tiled=True,
    ).astype(jnp.float32)
    out_rows = (sent.astype(jnp.float32) + wslot[:, None] * combined).astype(jnp.bfloat16)
    grad_rows = (cot_sent.astype(jnp.float32) + inward).astype(jnp.bfloat16)
    out_prev = from_behind(out_rows, "section", 1)
    grad_next = from_behind(grad_rows, "section", -1)
    next_input = pick_rows(route_prev, out_prev, tok_prev)
    prior_grad = pick_rows(route_next, grad_next, cot_next)
    return (next_input[None], prior_grad[None])


def solution(mesh):
    in_specs = (
        P("section", "expert", None),
        P("section", "expert", None),
        P("section", "expert", None),
        P("section", "expert", None),
        P("section", "expert", None),
        P("section", None, "expert"),
        P("section", None, "expert"),
        P("section", "expert", None),
    )
    out_specs = (P("section", "expert", None), P("section", "expert", None))
    return jax.shard_map(body, mesh=mesh, in_specs=in_specs, out_specs=out_specs, check_vma=False)
```

```python
import jax
import jax.numpy as jnp
from jax import lax
from jax.sharding import Mesh
from jax.sharding import PartitionSpec as P


CAP = 32
SWAP = [(0, 1), (1, 0)]


def from_behind(x, axis, by):
    length = lax.axis_size(axis)
    pairs = [(i, i + by) for i in range(length) if 0 <= i + by < length]
    return lax.ppermute(x, axis, pairs)


def silu_parts(gate):
    sig = jax.nn.sigmoid(gate)
    return (gate * sig, sig * (1.0 + gate * (1.0 - sig)))


def pick_rows(route, rows, bulk):
    taken = jnp.take(rows, jnp.maximum(route - 1, 0), axis=0)
    return jnp.where((route > 0)[:, None], taken, bulk)


def in_order(first, mine, other, axis):
    return jnp.where(first, jnp.stack([mine, other], axis), jnp.stack([other, mine], axis))


def gather_wide(x, first):
    own = lax.all_gather(x, "z", axis=0, tiled=True)
    other = lax.ppermute(own, "xlo", SWAP)
    zs = own.shape[0] // x.shape[0]
    rows = x.shape[0]
    both = in_order(first, own.reshape(zs, rows, -1), other.reshape(zs, rows, -1), 1)
    return both.reshape(zs * 2 * rows, -1)


def gather_narrow(x, first):
    other = lax.ppermute(x, "xlo", SWAP)
    pair = in_order(first, x, other, 0).reshape(2 * x.shape[0], -1)
    return lax.all_gather(pair, "z", axis=0, tiled=True)


def scatter_wide(q, first, rows):
    zs = q.shape[0] // (2 * rows)
    q = q.reshape(zs, 2, rows, -1)
    keep = jnp.where(first, q[:, 0], q[:, 1])
    give = jnp.where(first, q[:, 1], q[:, 0])
    got = lax.ppermute(give, "xlo", SWAP)
    total = (keep.astype(jnp.float32) + got.astype(jnp.float32)).astype(jnp.bfloat16)
    part = lax.psum_scatter(total.reshape(zs * rows, -1), "z", scatter_dimension=0, tiled=True)
    return part.astype(jnp.float32)


def scatter_narrow(q, first, rows):
    t = lax.psum_scatter(q, "z", scatter_dimension=0, tiled=True)
    t = t.reshape(2, rows, -1)
    keep = jnp.where(first, t[0], t[1])
    give = jnp.where(first, t[1], t[0])
    got = lax.ppermute(give, "xlo", SWAP)
    return keep.astype(jnp.float32) + got.astype(jnp.float32)


def body(
    tokens, cotangent, expert_ids, slot_index, gate_scale, gate_weight, up_weight, down_weight
):
    section = lax.axis_index("section")
    first = lax.axis_index("xlo") == 0
    local = tokens[0]
    grad_out = cotangent[0]
    named = expert_ids[0]
    gate_mat = gate_weight[0]
    up_mat = up_weight[0]
    down_mat = down_weight[0]
    width = local.shape[1]
    wide = (width // 7 * 4) // 128 * 128
    hit = named == section
    chosen = jnp.any(hit, axis=1)
    slot = jnp.sum(jnp.where(hit, slot_index[0], 0), axis=1)
    weight = jnp.sum(jnp.where(hit, gate_scale[0], jnp.float32(0.0)), axis=1)
    route = jnp.where(chosen, slot + 1, 0).astype(jnp.int32)

    tok_prev = from_behind(local, "section", 1)
    cot_next = from_behind(grad_out, "section", -1)
    route_prev = from_behind(route, "section", 1)
    route_next = from_behind(route, "section", -1)

    places = jnp.arange(CAP, dtype=jnp.int32)
    mask = (places[:, None] == slot[None, :]) & chosen[None, :]
    table = mask.astype(jnp.bfloat16)
    sent = jnp.dot(table, local, preferred_element_type=jnp.float32).astype(jnp.bfloat16)
    cot_sent = jnp.dot(table, grad_out, preferred_element_type=jnp.float32).astype(jnp.bfloat16)
    wslot = jnp.sum(jnp.where(mask, weight[None, :], jnp.float32(0.0)), axis=1)
    carried = (weight[:, None] * grad_out.astype(jnp.float32)).astype(jnp.bfloat16)
    back = jnp.dot(table, carried, preferred_element_type=jnp.float32).astype(jnp.bfloat16)

    sent_a = gather_wide(sent[:, :wide], first)
    back_a = gather_wide(back[:, :wide], first)
    sent_b = gather_narrow(sent[:, wide:], first)
    back_b = gather_narrow(back[:, wide:], first)

    f32 = jnp.float32
    gate = jnp.dot(sent_a, gate_mat[:wide], preferred_element_type=f32) + jnp.dot(
        sent_b, gate_mat[wide:], preferred_element_type=f32
    )
    up = jnp.dot(sent_a, up_mat[:wide], preferred_element_type=f32) + jnp.dot(
        sent_b, up_mat[wide:], preferred_element_type=f32
    )
    act, slope = silu_parts(gate)
    hidden = (act * up).astype(jnp.bfloat16)
    ahead_a = jnp.dot(hidden, down_mat[:, :wide], preferred_element_type=f32).astype(jnp.bfloat16)
    ahead_b = jnp.dot(hidden, down_mat[:, wide:], preferred_element_type=f32).astype(jnp.bfloat16)
    comb_b = scatter_narrow(ahead_b, first, CAP)
    grad_hidden = jnp.dot(back_a, down_mat[:, :wide].T, preferred_element_type=f32) + jnp.dot(
        back_b, down_mat[:, wide:].T, preferred_element_type=f32
    )
    grad_up = (grad_hidden * act).astype(jnp.bfloat16)
    grad_gate = (grad_hidden * up * slope).astype(jnp.bfloat16)
    behind_b = (
        jnp.dot(grad_gate, gate_mat[wide:].T, preferred_element_type=f32)
        + jnp.dot(grad_up, up_mat[wide:].T, preferred_element_type=f32)
    ).astype(jnp.bfloat16)
    behind_a = (
        jnp.dot(grad_gate, gate_mat[:wide].T, preferred_element_type=f32)
        + jnp.dot(grad_up, up_mat[:wide].T, preferred_element_type=f32)
    ).astype(jnp.bfloat16)
    comb_a = scatter_wide(ahead_a, first, CAP)
    inw_b = scatter_narrow(behind_b, first, CAP)
    inw_a = scatter_wide(behind_a, first, CAP)
    combined = jnp.concatenate([comb_a, comb_b], axis=1)
    inward = jnp.concatenate([inw_a, inw_b], axis=1)

    out_rows = (sent.astype(f32) + wslot[:, None] * combined).astype(jnp.bfloat16)
    grad_rows = (cot_sent.astype(f32) + inward).astype(jnp.bfloat16)
    out_prev = from_behind(out_rows, "section", 1)
    grad_next = from_behind(grad_rows, "section", -1)
    next_input = pick_rows(route_prev, out_prev, tok_prev)
    prior_grad = pick_rows(route_next, grad_next, cot_next)
    return (next_input[None], prior_grad[None])


def solution(mesh):
    sections, experts = mesh.devices.shape
    grid = Mesh(mesh.devices.reshape(sections, 2, experts // 2), ("section", "xlo", "z"))
    ex = ("xlo", "z")
    in_specs = (
        P("section", ex, None),
        P("section", ex, None),
        P("section", ex, None),
        P("section", ex, None),
        P("section", ex, None),
        P("section", None, ex),
        P("section", None, ex),
        P("section", ex, None),
    )
    out_specs = (P("section", ex, None), P("section", ex, None))

    return jax.shard_map(body, mesh=grid, in_specs=in_specs, out_specs=out_specs, check_vma=False)
```

```python
import jax
import jax.numpy as jnp
from jax import lax
from jax.sharding import PartitionSpec as P


CAP = 32


def from_behind(x, axis, by):
    length = lax.axis_size(axis)
    pairs = [(i, i + by) for i in range(length) if 0 <= i + by < length]
    return lax.ppermute(x, axis, pairs)


def silu_parts(gate):
    sig = jax.nn.sigmoid(gate)
    return (gate * sig, sig * (1.0 + gate * (1.0 - sig)))


def pick_rows(route, rows, bulk):
    taken = jnp.take(rows, jnp.maximum(route - 1, 0), axis=0)
    return jnp.where((route > 0)[:, None], taken, bulk)


def body(
    tokens, cotangent, expert_ids, slot_index, gate_scale, gate_weight, up_weight, down_weight
):
    section = lax.axis_index("section")
    local = tokens[0]
    grad_out = cotangent[0]
    named = expert_ids[0]
    gate_mat = gate_weight[0]
    up_mat = up_weight[0]
    down_mat = down_weight[0]
    width_local = gate_mat.shape[1]
    hit = named == section
    chosen = jnp.any(hit, axis=1)
    slot = jnp.sum(jnp.where(hit, slot_index[0], 0), axis=1)
    weight = jnp.sum(jnp.where(hit, gate_scale[0], jnp.float32(0.0)), axis=1)
    route = jnp.where(chosen, slot + 1, 0).astype(jnp.int32)

    tok_prev = from_behind(local, "section", 1)
    cot_next = from_behind(grad_out, "section", -1)
    route_prev = from_behind(route, "section", 1)
    route_next = from_behind(route, "section", -1)

    places = jnp.arange(CAP, dtype=jnp.int32)
    mask = (places[:, None] == slot[None, :]) & chosen[None, :]
    table = mask.astype(jnp.bfloat16)
    sent = jnp.dot(table, local, preferred_element_type=jnp.float32).astype(jnp.bfloat16)
    cot_sent = jnp.dot(table, grad_out, preferred_element_type=jnp.float32).astype(jnp.bfloat16)
    wslot = jnp.sum(jnp.where(mask, weight[None, :], jnp.float32(0.0)), axis=1)
    carried = (weight[:, None] * grad_out.astype(jnp.float32)).astype(jnp.bfloat16)
    back = jnp.dot(table, carried, preferred_element_type=jnp.float32).astype(jnp.bfloat16)
    both = lax.all_gather(jnp.concatenate([sent, back], axis=1), "expert", axis=0, tiled=True)
    width = local.shape[1]
    piece = both[:, :width]
    piece_back = both[:, width:]
    gate_up = jnp.concatenate(
        [
            jnp.dot(piece, gate_mat, preferred_element_type=jnp.float32),
            jnp.dot(piece, up_mat, preferred_element_type=jnp.float32),
        ],
        axis=1,
    )
    gate = gate_up[:, :width_local]
    up = gate_up[:, width_local:]
    act, slope = silu_parts(gate)
    hidden = (act * up).astype(jnp.bfloat16)
    ahead = jnp.dot(hidden, down_mat, preferred_element_type=jnp.float32).astype(jnp.bfloat16)
    grad_hidden = jnp.dot(piece_back, down_mat.T, preferred_element_type=jnp.float32)
    grad_up = (grad_hidden * act).astype(jnp.bfloat16)
    grad_gate = (grad_hidden * up * slope).astype(jnp.bfloat16)
    behind = jnp.dot(grad_gate, gate_mat.T, preferred_element_type=jnp.float32)
    behind = (behind + jnp.dot(grad_up, up_mat.T, preferred_element_type=jnp.float32)).astype(
        jnp.bfloat16
    )
    sums = lax.psum_scatter(
        jnp.concatenate([ahead, behind], axis=1), "expert", scatter_dimension=0, tiled=True
    )
    combined = sums[:, :width].astype(jnp.float32)
    inward = sums[:, width:].astype(jnp.float32)
    out_rows = (sent.astype(jnp.float32) + wslot[:, None] * combined).astype(jnp.bfloat16)
    grad_rows = (cot_sent.astype(jnp.float32) + inward).astype(jnp.bfloat16)
    out_prev = from_behind(out_rows, "section", 1)
    grad_next = from_behind(grad_rows, "section", -1)
    next_input = pick_rows(route_prev, out_prev, tok_prev)
    prior_grad = pick_rows(route_next, grad_next, cot_next)
    return (next_input[None], prior_grad[None])


def solution(mesh):
    in_specs = (
        P("section", "expert", None),
        P("section", "expert", None),
        P("section", "expert", None),
        P("section", "expert", None),
        P("section", "expert", None),
        P("section", None, "expert"),
        P("section", None, "expert"),
        P("section", "expert", None),
    )
    out_specs = (P("section", "expert", None), P("section", "expert", None))

    return jax.shard_map(body, mesh=mesh, in_specs=in_specs, out_specs=out_specs, check_vma=False)
```

```python
import jax
import jax.numpy as jnp
from jax import lax
from jax.sharding import PartitionSpec as P


CAP = 32


def from_behind(x, axis, by):
    length = lax.axis_size(axis)
    pairs = [(i, i + by) for i in range(length) if 0 <= i + by < length]
    return lax.ppermute(x, axis, pairs)


def silu_parts(gate):
    sig = jax.nn.sigmoid(gate)
    return (gate * sig, sig * (1.0 + gate * (1.0 - sig)))


def pick_rows(route, rows, bulk):
    places = jnp.arange(1, rows.shape[0] + 1, dtype=jnp.int32)
    table = (route[:, None] == places[None, :]).astype(rows.dtype)
    taken = jnp.dot(table, rows, preferred_element_type=jnp.float32).astype(rows.dtype)
    return jnp.where((route > 0)[:, None], taken, bulk)


def body(
    tokens, cotangent, expert_ids, slot_index, gate_scale, gate_weight, up_weight, down_weight
):
    section = lax.axis_index("section")
    local = tokens[0]
    grad_out = cotangent[0]
    named = expert_ids[0]
    gate_mat = gate_weight[0]
    up_mat = up_weight[0]
    down_mat = down_weight[0]
    width_local = gate_mat.shape[1]
    hit = named == section
    chosen = jnp.any(hit, axis=1)
    slot = jnp.sum(jnp.where(hit, slot_index[0], 0), axis=1)
    weight = jnp.sum(jnp.where(hit, gate_scale[0], jnp.float32(0.0)), axis=1)
    route = jnp.where(chosen, slot + 1, 0).astype(jnp.int32)

    tok_prev = from_behind(local, "section", 1)
    cot_next = from_behind(grad_out, "section", -1)
    route_prev = from_behind(route, "section", 1)
    route_next = from_behind(route, "section", -1)

    places = jnp.arange(CAP, dtype=jnp.int32)
    mask = (places[:, None] == slot[None, :]) & chosen[None, :]
    table = mask.astype(jnp.bfloat16)
    sent = jnp.dot(table, local, preferred_element_type=jnp.float32).astype(jnp.bfloat16)
    cot_sent = jnp.dot(table, grad_out, preferred_element_type=jnp.float32).astype(jnp.bfloat16)
    wslot = jnp.sum(jnp.where(mask, weight[None, :], jnp.float32(0.0)), axis=1)
    carried = (weight[:, None] * grad_out.astype(jnp.float32)).astype(jnp.bfloat16)
    back = jnp.dot(table, carried, preferred_element_type=jnp.float32).astype(jnp.bfloat16)
    piece = lax.all_gather(sent, "expert", axis=0, tiled=True)
    piece_back = lax.all_gather(back, "expert", axis=0, tiled=True)
    gate_up = jnp.concatenate(
        [
            jnp.dot(piece, gate_mat, preferred_element_type=jnp.float32),
            jnp.dot(piece, up_mat, preferred_element_type=jnp.float32),
        ],
        axis=1,
    )
    gate = gate_up[:, :width_local]
    up = gate_up[:, width_local:]
    act, slope = silu_parts(gate)
    hidden = (act * up).astype(jnp.bfloat16)
    ahead = jnp.dot(hidden, down_mat, preferred_element_type=jnp.float32).astype(jnp.bfloat16)
    combined = lax.psum_scatter(ahead, "expert", scatter_dimension=0, tiled=True)
    combined = combined.astype(jnp.float32)
    grad_hidden = jnp.dot(piece_back, down_mat.T, preferred_element_type=jnp.float32)
    grad_up = (grad_hidden * act).astype(jnp.bfloat16)
    grad_gate = (grad_hidden * up * slope).astype(jnp.bfloat16)
    behind = jnp.dot(grad_gate, gate_mat.T, preferred_element_type=jnp.float32)
    behind = (behind + jnp.dot(grad_up, up_mat.T, preferred_element_type=jnp.float32)).astype(
        jnp.bfloat16
    )
    inward = lax.psum_scatter(behind, "expert", scatter_dimension=0, tiled=True)
    inward = inward.astype(jnp.float32)
    out_rows = (sent.astype(jnp.float32) + wslot[:, None] * combined).astype(jnp.bfloat16)
    grad_rows = (cot_sent.astype(jnp.float32) + inward).astype(jnp.bfloat16)
    out_prev = from_behind(out_rows, "section", 1)
    grad_next = from_behind(grad_rows, "section", -1)
    next_input = pick_rows(route_prev, out_prev, tok_prev)
    prior_grad = pick_rows(route_next, grad_next, cot_next)
    return (next_input[None], prior_grad[None])


def solution(mesh):
    in_specs = (
        P("section", "expert", None),
        P("section", "expert", None),
        P("section", "expert", None),
        P("section", "expert", None),
        P("section", "expert", None),
        P("section", None, "expert"),
        P("section", None, "expert"),
        P("section", "expert", None),
    )
    out_specs = (P("section", "expert", None), P("section", "expert", None))

    return jax.shard_map(body, mesh=mesh, in_specs=in_specs, out_specs=out_specs, check_vma=False)
```

```python
import jax
import jax.numpy as jnp
from jax import lax
from jax.sharding import Mesh
from jax.sharding import PartitionSpec as P


CAP = 32
SWAP = [(0, 1), (1, 0)]


def from_behind(x, axis, by):
    length = lax.axis_size(axis)
    pairs = [(i, i + by) for i in range(length) if 0 <= i + by < length]
    return lax.ppermute(x, axis, pairs)


def silu_parts(gate):
    sig = jax.nn.sigmoid(gate)
    return (gate * sig, sig * (1.0 + gate * (1.0 - sig)))


def pick_rows(route, rows, bulk):
    places = jnp.arange(1, rows.shape[0] + 1, dtype=jnp.int32)
    table = (route[:, None] == places[None, :]).astype(rows.dtype)
    taken = jnp.dot(table, rows, preferred_element_type=jnp.float32).astype(rows.dtype)
    return jnp.where((route > 0)[:, None], taken, bulk)


def in_order(first, mine, other, axis):
    return jnp.where(first, jnp.stack([mine, other], axis), jnp.stack([other, mine], axis))


def gather_wide(x, first):
    own = lax.all_gather(x, "z", axis=0, tiled=True)
    other = lax.ppermute(own, "xlo", SWAP)
    zs = own.shape[0] // x.shape[0]
    rows = x.shape[0]
    both = in_order(first, own.reshape(zs, rows, -1), other.reshape(zs, rows, -1), 1)
    return both.reshape(zs * 2 * rows, -1)


def gather_narrow(x, first):
    other = lax.ppermute(x, "xlo", SWAP)
    pair = in_order(first, x, other, 0).reshape(2 * x.shape[0], -1)
    return lax.all_gather(pair, "z", axis=0, tiled=True)


def scatter_wide(q, first, rows):
    zs = q.shape[0] // (2 * rows)
    q = q.reshape(zs, 2, rows, -1)
    keep = jnp.where(first, q[:, 0], q[:, 1])
    give = jnp.where(first, q[:, 1], q[:, 0])
    got = lax.ppermute(give, "xlo", SWAP)
    total = (keep.astype(jnp.float32) + got.astype(jnp.float32)).astype(jnp.bfloat16)
    part = lax.psum_scatter(total.reshape(zs * rows, -1), "z", scatter_dimension=0, tiled=True)
    return part.astype(jnp.float32)


def scatter_narrow(q, first, rows):
    t = lax.psum_scatter(q, "z", scatter_dimension=0, tiled=True)
    t = t.reshape(2, rows, -1)
    keep = jnp.where(first, t[0], t[1])
    give = jnp.where(first, t[1], t[0])
    got = lax.ppermute(give, "xlo", SWAP)
    return keep.astype(jnp.float32) + got.astype(jnp.float32)


def body(
    tokens, cotangent, expert_ids, slot_index, gate_scale, gate_weight, up_weight, down_weight
):
    section = lax.axis_index("section")
    first = lax.axis_index("xlo") == 0
    local = tokens[0]
    grad_out = cotangent[0]
    named = expert_ids[0]
    gate_mat = gate_weight[0]
    up_mat = up_weight[0]
    down_mat = down_weight[0]
    width = local.shape[1]
    wide = (width // 7 * 4) // 128 * 128
    hit = named == section
    chosen = jnp.any(hit, axis=1)
    slot = jnp.sum(jnp.where(hit, slot_index[0], 0), axis=1)
    weight = jnp.sum(jnp.where(hit, gate_scale[0], jnp.float32(0.0)), axis=1)
    route = jnp.where(chosen, slot + 1, 0).astype(jnp.int32)

    tok_prev = from_behind(local, "section", 1)
    cot_next = from_behind(grad_out, "section", -1)
    route_prev = from_behind(route, "section", 1)
    route_next = from_behind(route, "section", -1)

    places = jnp.arange(CAP, dtype=jnp.int32)
    mask = (places[:, None] == slot[None, :]) & chosen[None, :]
    table = mask.astype(jnp.bfloat16)
    sent = jnp.dot(table, local, preferred_element_type=jnp.float32).astype(jnp.bfloat16)
    cot_sent = jnp.dot(table, grad_out, preferred_element_type=jnp.float32).astype(jnp.bfloat16)
    wslot = jnp.sum(jnp.where(mask, weight[None, :], jnp.float32(0.0)), axis=1)
    carried = (weight[:, None] * grad_out.astype(jnp.float32)).astype(jnp.bfloat16)
    back = jnp.dot(table, carried, preferred_element_type=jnp.float32).astype(jnp.bfloat16)

    narrow = width - wide
    both_a = gather_wide(jnp.concatenate([sent[:, :wide], back[:, :wide]], axis=1), first)
    both_b = gather_narrow(jnp.concatenate([sent[:, wide:], back[:, wide:]], axis=1), first)
    sent_a, back_a = both_a[:, :wide], both_a[:, wide:]
    sent_b, back_b = both_b[:, :narrow], both_b[:, narrow:]

    f32 = jnp.float32
    gate = jnp.dot(sent_a, gate_mat[:wide], preferred_element_type=f32) + jnp.dot(
        sent_b, gate_mat[wide:], preferred_element_type=f32
    )
    up = jnp.dot(sent_a, up_mat[:wide], preferred_element_type=f32) + jnp.dot(
        sent_b, up_mat[wide:], preferred_element_type=f32
    )
    act, slope = silu_parts(gate)
    hidden = (act * up).astype(jnp.bfloat16)
    ahead_a = jnp.dot(hidden, down_mat[:, :wide], preferred_element_type=f32).astype(jnp.bfloat16)
    ahead_b = jnp.dot(hidden, down_mat[:, wide:], preferred_element_type=f32).astype(jnp.bfloat16)
    comb_b = scatter_narrow(ahead_b, first, CAP)
    grad_hidden = jnp.dot(back_a, down_mat[:, :wide].T, preferred_element_type=f32) + jnp.dot(
        back_b, down_mat[:, wide:].T, preferred_element_type=f32
    )
    grad_up = (grad_hidden * act).astype(jnp.bfloat16)
    grad_gate = (grad_hidden * up * slope).astype(jnp.bfloat16)
    behind_b = (
        jnp.dot(grad_gate, gate_mat[wide:].T, preferred_element_type=f32)
        + jnp.dot(grad_up, up_mat[wide:].T, preferred_element_type=f32)
    ).astype(jnp.bfloat16)
    behind_a = (
        jnp.dot(grad_gate, gate_mat[:wide].T, preferred_element_type=f32)
        + jnp.dot(grad_up, up_mat[:wide].T, preferred_element_type=f32)
    ).astype(jnp.bfloat16)
    comb_a = scatter_wide(ahead_a, first, CAP)
    inw_b = scatter_narrow(behind_b, first, CAP)
    inw_a = scatter_wide(behind_a, first, CAP)
    combined = jnp.concatenate([comb_a, comb_b], axis=1)
    inward = jnp.concatenate([inw_a, inw_b], axis=1)

    out_rows = (sent.astype(f32) + wslot[:, None] * combined).astype(jnp.bfloat16)
    grad_rows = (cot_sent.astype(f32) + inward).astype(jnp.bfloat16)
    out_prev = from_behind(out_rows, "section", 1)
    grad_next = from_behind(grad_rows, "section", -1)
    next_input = pick_rows(route_prev, out_prev, tok_prev)
    prior_grad = pick_rows(route_next, grad_next, cot_next)
    return (next_input[None], prior_grad[None])


def solution(mesh):
    sections, experts = mesh.devices.shape
    grid = Mesh(mesh.devices.reshape(sections, 2, experts // 2), ("section", "xlo", "z"))
    ex = ("xlo", "z")
    in_specs = (
        P("section", ex, None),
        P("section", ex, None),
        P("section", ex, None),
        P("section", ex, None),
        P("section", ex, None),
        P("section", None, ex),
        P("section", None, ex),
        P("section", ex, None),
    )
    out_specs = (P("section", ex, None), P("section", ex, None))

    return jax.shard_map(body, mesh=grid, in_specs=in_specs, out_specs=out_specs, check_vma=False)
```

```python
import jax
import jax.numpy as jnp
from jax import lax
from jax.sharding import Mesh
from jax.sharding import PartitionSpec as P


CAP = 32
SWAP = [(0, 1), (1, 0)]


def from_behind(x, axis, by):
    length = lax.axis_size(axis)
    pairs = [(i, i + by) for i in range(length) if 0 <= i + by < length]
    return lax.ppermute(x, axis, pairs)


def silu_parts(gate):
    sig = jax.nn.sigmoid(gate)
    return (gate * sig, sig * (1.0 + gate * (1.0 - sig)))


def pick_rows(route, rows, bulk):
    places = jnp.arange(1, rows.shape[0] + 1, dtype=jnp.int32)
    table = (route[:, None] == places[None, :]).astype(rows.dtype)
    taken = jnp.dot(table, rows, preferred_element_type=jnp.float32).astype(rows.dtype)
    return jnp.where((route > 0)[:, None], taken, bulk)


def in_order(first, mine, other, axis):
    return jnp.where(first, jnp.stack([mine, other], axis), jnp.stack([other, mine], axis))


def gather_wide(x, first):
    own = lax.all_gather(x, "z", axis=0, tiled=True)
    other = lax.ppermute(own, "xlo", SWAP)
    zs = own.shape[0] // x.shape[0]
    rows = x.shape[0]
    both = in_order(first, own.reshape(zs, rows, -1), other.reshape(zs, rows, -1), 1)
    return both.reshape(zs * 2 * rows, -1)


def gather_narrow(x, first):
    other = lax.ppermute(x, "xlo", SWAP)
    pair = in_order(first, x, other, 0).reshape(2 * x.shape[0], -1)
    return lax.all_gather(pair, "z", axis=0, tiled=True)


def scatter_wide(qs, first, rows):
    totals = []
    for q in qs:
        zs = q.shape[0] // (2 * rows)
        q = q.reshape(zs, 2, rows, -1)
        keep = jnp.where(first, q[:, 0], q[:, 1])
        give = jnp.where(first, q[:, 1], q[:, 0])
        got = lax.ppermute(give, "xlo", SWAP)
        total = (keep.astype(jnp.float32) + got.astype(jnp.float32)).astype(jnp.bfloat16)
        totals.append(total.reshape(zs * rows, -1))
    part = lax.psum_scatter(
        jnp.concatenate(totals, axis=1), "z", scatter_dimension=0, tiled=True
    ).astype(jnp.float32)
    cut = totals[0].shape[1]
    return part[:, :cut], part[:, cut:]


def scatter_narrow(q, first, rows):
    t = lax.psum_scatter(q, "z", scatter_dimension=0, tiled=True)
    t = t.reshape(2, rows, -1)
    keep = jnp.where(first, t[0], t[1])
    give = jnp.where(first, t[1], t[0])
    got = lax.ppermute(give, "xlo", SWAP)
    return keep.astype(jnp.float32) + got.astype(jnp.float32)


def body(
    tokens, cotangent, expert_ids, slot_index, gate_scale, gate_weight, up_weight, down_weight
):
    section = lax.axis_index("section")
    first = lax.axis_index("xlo") == 0
    local = tokens[0]
    grad_out = cotangent[0]
    named = expert_ids[0]
    gate_mat = gate_weight[0]
    up_mat = up_weight[0]
    down_mat = down_weight[0]
    width = local.shape[1]
    wide = (width // 2) // 128 * 128
    wide_r = (width // 7 * 4) // 128 * 128
    hit = named == section
    chosen = jnp.any(hit, axis=1)
    slot = jnp.sum(jnp.where(hit, slot_index[0], 0), axis=1)
    weight = jnp.sum(jnp.where(hit, gate_scale[0], jnp.float32(0.0)), axis=1)
    route = jnp.where(chosen, slot + 1, 0).astype(jnp.int32)

    tok_prev = from_behind(local, "section", 1)
    cot_next = from_behind(grad_out, "section", -1)
    route_prev = from_behind(route, "section", 1)
    route_next = from_behind(route, "section", -1)

    places = jnp.arange(CAP, dtype=jnp.int32)
    mask = (places[:, None] == slot[None, :]) & chosen[None, :]
    table = mask.astype(jnp.bfloat16)
    sent = jnp.dot(table, local, preferred_element_type=jnp.float32).astype(jnp.bfloat16)
    cot_sent = jnp.dot(table, grad_out, preferred_element_type=jnp.float32).astype(jnp.bfloat16)
    wslot = jnp.sum(jnp.where(mask, weight[None, :], jnp.float32(0.0)), axis=1)
    carried = (weight[:, None] * grad_out.astype(jnp.float32)).astype(jnp.bfloat16)
    back = jnp.dot(table, carried, preferred_element_type=jnp.float32).astype(jnp.bfloat16)

    narrow = width - wide
    both_a = gather_wide(jnp.concatenate([sent[:, :wide], back[:, :wide]], axis=1), first)
    both_b = gather_narrow(jnp.concatenate([sent[:, wide:], back[:, wide:]], axis=1), first)
    sent_a, back_a = both_a[:, :wide], both_a[:, wide:]
    sent_b, back_b = both_b[:, :narrow], both_b[:, narrow:]

    f32 = jnp.float32
    gate = jnp.dot(sent_a, gate_mat[:wide], preferred_element_type=f32) + jnp.dot(
        sent_b, gate_mat[wide:], preferred_element_type=f32
    )
    up = jnp.dot(sent_a, up_mat[:wide], preferred_element_type=f32) + jnp.dot(
        sent_b, up_mat[wide:], preferred_element_type=f32
    )
    act, slope = silu_parts(gate)
    hidden = (act * up).astype(jnp.bfloat16)
    ahead_a = jnp.dot(hidden, down_mat[:, :wide_r], preferred_element_type=f32).astype(jnp.bfloat16)
    ahead_b = jnp.dot(hidden, down_mat[:, wide_r:], preferred_element_type=f32).astype(jnp.bfloat16)
    comb_b = scatter_narrow(ahead_b, first, CAP)
    grad_hidden = jnp.dot(back_a, down_mat[:, :wide].T, preferred_element_type=f32) + jnp.dot(
        back_b, down_mat[:, wide:].T, preferred_element_type=f32
    )
    grad_up = (grad_hidden * act).astype(jnp.bfloat16)
    grad_gate = (grad_hidden * up * slope).astype(jnp.bfloat16)
    behind_b = (
        jnp.dot(grad_gate, gate_mat[wide_r:].T, preferred_element_type=f32)
        + jnp.dot(grad_up, up_mat[wide_r:].T, preferred_element_type=f32)
    ).astype(jnp.bfloat16)
    behind_a = (
        jnp.dot(grad_gate, gate_mat[:wide_r].T, preferred_element_type=f32)
        + jnp.dot(grad_up, up_mat[:wide_r].T, preferred_element_type=f32)
    ).astype(jnp.bfloat16)
    inw_b = scatter_narrow(behind_b, first, CAP)
    comb_a, inw_a = scatter_wide([ahead_a, behind_a], first, CAP)
    combined = jnp.concatenate([comb_a, comb_b], axis=1)
    inward = jnp.concatenate([inw_a, inw_b], axis=1)

    out_rows = (sent.astype(f32) + wslot[:, None] * combined).astype(jnp.bfloat16)
    grad_rows = (cot_sent.astype(f32) + inward).astype(jnp.bfloat16)
    out_prev = from_behind(out_rows, "section", 1)
    grad_next = from_behind(grad_rows, "section", -1)
    next_input = pick_rows(route_prev, out_prev, tok_prev)
    prior_grad = pick_rows(route_next, grad_next, cot_next)
    return (next_input[None], prior_grad[None])


def solution(mesh):
    sections, experts = mesh.devices.shape
    grid = Mesh(mesh.devices.reshape(sections, 2, experts // 2), ("section", "xlo", "z"))
    ex = ("xlo", "z")
    in_specs = (
        P("section", ex, None),
        P("section", ex, None),
        P("section", ex, None),
        P("section", ex, None),
        P("section", ex, None),
        P("section", None, ex),
        P("section", None, ex),
        P("section", ex, None),
    )
    out_specs = (P("section", ex, None), P("section", ex, None))

    return jax.shard_map(body, mesh=grid, in_specs=in_specs, out_specs=out_specs, check_vma=False)
```

```python
import jax
import jax.numpy as jnp
from jax import lax
from jax.sharding import Mesh
from jax.sharding import PartitionSpec as P


CAP = 32
SWAP = [(0, 1), (1, 0)]


def from_behind(x, axis, by):
    length = lax.axis_size(axis)
    pairs = [(i, i + by) for i in range(length) if 0 <= i + by < length]
    return lax.ppermute(x, axis, pairs)


def silu_parts(gate):
    sig = jax.nn.sigmoid(gate)
    return (gate * sig, sig * (1.0 + gate * (1.0 - sig)))


def pick_rows(route, rows, bulk):
    places = jnp.arange(1, rows.shape[0] + 1, dtype=jnp.int32)
    table = (route[:, None] == places[None, :]).astype(rows.dtype)
    taken = jnp.dot(table, rows, preferred_element_type=jnp.float32).astype(rows.dtype)
    return jnp.where((route > 0)[:, None], taken, bulk)


def in_order(first, mine, other, axis):
    return jnp.where(first, jnp.stack([mine, other], axis), jnp.stack([other, mine], axis))


def gather_wide(x, first):
    own = lax.all_gather(x, "z", axis=0, tiled=True)
    other = lax.ppermute(own, "xlo", SWAP)
    zs = own.shape[0] // x.shape[0]
    rows = x.shape[0]
    both = in_order(first, own.reshape(zs, rows, -1), other.reshape(zs, rows, -1), 1)
    return both.reshape(zs * 2 * rows, -1)


def gather_narrow(x, first):
    other = lax.ppermute(x, "xlo", SWAP)
    pair = in_order(first, x, other, 0).reshape(2 * x.shape[0], -1)
    return lax.all_gather(pair, "z", axis=0, tiled=True)


def scatter_wide(q, first, rows):
    zs = q.shape[0] // (2 * rows)
    q = q.reshape(zs, 2, rows, -1)
    keep = jnp.where(first, q[:, 0], q[:, 1])
    give = jnp.where(first, q[:, 1], q[:, 0])
    got = lax.ppermute(give, "xlo", SWAP)
    total = (keep.astype(jnp.float32) + got.astype(jnp.float32)).astype(jnp.bfloat16)
    part = lax.psum_scatter(total.reshape(zs * rows, -1), "z", scatter_dimension=0, tiled=True)
    return part.astype(jnp.float32)


def scatter_narrow(q, first, rows):
    t = lax.psum_scatter(q, "z", scatter_dimension=0, tiled=True)
    t = t.reshape(2, rows, -1)
    keep = jnp.where(first, t[0], t[1])
    give = jnp.where(first, t[1], t[0])
    got = lax.ppermute(give, "xlo", SWAP)
    return keep.astype(jnp.float32) + got.astype(jnp.float32)


def body(
    tokens, cotangent, expert_ids, slot_index, gate_scale, gate_weight, up_weight, down_weight
):
    section = lax.axis_index("section")
    first = lax.axis_index("xlo") == 0
    local = tokens[0]
    grad_out = cotangent[0]
    named = expert_ids[0]
    gate_mat = gate_weight[0]
    up_mat = up_weight[0]
    down_mat = down_weight[0]
    width = local.shape[1]
    wide = (width // 2) // 128 * 128
    wide_r = (width // 7 * 4) // 128 * 128
    hit = named == section
    chosen = jnp.any(hit, axis=1)
    slot = jnp.sum(jnp.where(hit, slot_index[0], 0), axis=1)
    weight = jnp.sum(jnp.where(hit, gate_scale[0], jnp.float32(0.0)), axis=1)
    route = jnp.where(chosen, slot + 1, 0).astype(jnp.int32)

    tok_prev = from_behind(local, "section", 1)
    cot_next = from_behind(grad_out, "section", -1)
    route_prev = from_behind(route, "section", 1)
    route_next = from_behind(route, "section", -1)

    places = jnp.arange(CAP, dtype=jnp.int32)
    mask = (places[:, None] == slot[None, :]) & chosen[None, :]
    table = mask.astype(jnp.bfloat16)
    sent = jnp.dot(table, local, preferred_element_type=jnp.float32).astype(jnp.bfloat16)
    cot_sent = jnp.dot(table, grad_out, preferred_element_type=jnp.float32).astype(jnp.bfloat16)
    wslot = jnp.sum(jnp.where(mask, weight[None, :], jnp.float32(0.0)), axis=1)
    carried = (weight[:, None] * grad_out.astype(jnp.float32)).astype(jnp.bfloat16)
    back = jnp.dot(table, carried, preferred_element_type=jnp.float32).astype(jnp.bfloat16)

    narrow = width - wide
    both_a = gather_wide(jnp.concatenate([sent[:, :wide], back[:, :wide]], axis=1), first)
    both_b = gather_narrow(jnp.concatenate([sent[:, wide:], back[:, wide:]], axis=1), first)
    sent_a, back_a = both_a[:, :wide], both_a[:, wide:]
    sent_b, back_b = both_b[:, :narrow], both_b[:, narrow:]

    f32 = jnp.float32
    gate = jnp.dot(sent_a, gate_mat[:wide], preferred_element_type=f32) + jnp.dot(
        sent_b, gate_mat[wide:], preferred_element_type=f32
    )
    up = jnp.dot(sent_a, up_mat[:wide], preferred_element_type=f32) + jnp.dot(
        sent_b, up_mat[wide:], preferred_element_type=f32
    )
    act, slope = silu_parts(gate)
    hidden = (act * up).astype(jnp.bfloat16)
    ahead_a = jnp.dot(hidden, down_mat[:, :wide_r], preferred_element_type=f32).astype(jnp.bfloat16)
    ahead_b = jnp.dot(hidden, down_mat[:, wide_r:], preferred_element_type=f32).astype(jnp.bfloat16)
    comb_b = scatter_narrow(ahead_b, first, CAP)
    grad_hidden = jnp.dot(back_a, down_mat[:, :wide].T, preferred_element_type=f32) + jnp.dot(
        back_b, down_mat[:, wide:].T, preferred_element_type=f32
    )
    grad_up = (grad_hidden * act).astype(jnp.bfloat16)
    grad_gate = (grad_hidden * up * slope).astype(jnp.bfloat16)
    behind_b = (
        jnp.dot(grad_gate, gate_mat[wide_r:].T, preferred_element_type=f32)
        + jnp.dot(grad_up, up_mat[wide_r:].T, preferred_element_type=f32)
    ).astype(jnp.bfloat16)
    behind_a = (
        jnp.dot(grad_gate, gate_mat[:wide_r].T, preferred_element_type=f32)
        + jnp.dot(grad_up, up_mat[:wide_r].T, preferred_element_type=f32)
    ).astype(jnp.bfloat16)
    comb_a = scatter_wide(ahead_a, first, CAP)
    inw_b = scatter_narrow(behind_b, first, CAP)
    inw_a = scatter_wide(behind_a, first, CAP)
    combined = jnp.concatenate([comb_a, comb_b], axis=1)
    inward = jnp.concatenate([inw_a, inw_b], axis=1)

    out_rows = (sent.astype(f32) + wslot[:, None] * combined).astype(jnp.bfloat16)
    grad_rows = (cot_sent.astype(f32) + inward).astype(jnp.bfloat16)
    out_prev = from_behind(out_rows, "section", 1)
    grad_next = from_behind(grad_rows, "section", -1)
    next_input = pick_rows(route_prev, out_prev, tok_prev)
    prior_grad = pick_rows(route_next, grad_next, cot_next)
    return (next_input[None], prior_grad[None])


def solution(mesh):
    sections, experts = mesh.devices.shape
    grid = Mesh(mesh.devices.reshape(sections, 2, experts // 2), ("section", "xlo", "z"))
    ex = ("xlo", "z")
    in_specs = (
        P("section", ex, None),
        P("section", ex, None),
        P("section", ex, None),
        P("section", ex, None),
        P("section", ex, None),
        P("section", None, ex),
        P("section", None, ex),
        P("section", ex, None),
    )
    out_specs = (P("section", ex, None), P("section", ex, None))

    return jax.shard_map(body, mesh=grid, in_specs=in_specs, out_specs=out_specs, check_vma=False)
```

```python
import jax
import jax.numpy as jnp
from jax import lax
from jax.sharding import Mesh
from jax.sharding import PartitionSpec as P


CAP = 32
SWAP = [(0, 1), (1, 0)]


def from_behind(x, axis, by):
    length = lax.axis_size(axis)
    pairs = [(i, i + by) for i in range(length) if 0 <= i + by < length]
    return lax.ppermute(x, axis, pairs)


def silu_parts(gate):
    sig = jax.nn.sigmoid(gate)
    return (gate * sig, sig * (1.0 + gate * (1.0 - sig)))


def pick_rows(route, rows, bulk):
    places = jnp.arange(1, rows.shape[0] + 1, dtype=jnp.int32)
    table = (route[:, None] == places[None, :]).astype(rows.dtype)
    taken = jnp.dot(table, rows, preferred_element_type=jnp.float32).astype(rows.dtype)
    return jnp.where((route > 0)[:, None], taken, bulk)


def in_order(first, mine, other, axis):
    return jnp.where(first, jnp.stack([mine, other], axis), jnp.stack([other, mine], axis))


def gather_wide(x):
    own = lax.all_gather(x, "z", axis=0, tiled=True)
    other = lax.ppermute(own, "xlo", SWAP)
    return own, other


def gather_narrow(x, first):
    other = lax.ppermute(x, "xlo", SWAP)
    pair = in_order(first, x, other, 0).reshape(2 * x.shape[0], -1)
    return lax.all_gather(pair, "z", axis=0, tiled=True)


def scatter_wide(q, first, rows):
    zs = q.shape[0] // (2 * rows)
    q = q.reshape(zs, 2, rows, -1)
    keep = jnp.where(first, q[:, 0], q[:, 1])
    give = jnp.where(first, q[:, 1], q[:, 0])
    got = lax.ppermute(give, "xlo", SWAP)
    total = (keep.astype(jnp.float32) + got.astype(jnp.float32)).astype(jnp.bfloat16)
    part = lax.psum_scatter(total.reshape(zs * rows, -1), "z", scatter_dimension=0, tiled=True)
    return part.astype(jnp.float32)


def scatter_narrow(q, first, rows):
    t = lax.psum_scatter(q, "z", scatter_dimension=0, tiled=True)
    t = t.reshape(2, rows, -1)
    keep = jnp.where(first, t[0], t[1])
    give = jnp.where(first, t[1], t[0])
    got = lax.ppermute(give, "xlo", SWAP)
    return keep.astype(jnp.float32) + got.astype(jnp.float32)


def body(
    tokens, cotangent, expert_ids, slot_index, gate_scale, gate_weight, up_weight, down_weight
):
    section = lax.axis_index("section")
    first = lax.axis_index("xlo") == 0
    local = tokens[0]
    grad_out = cotangent[0]
    named = expert_ids[0]
    gate_mat = gate_weight[0]
    up_mat = up_weight[0]
    down_mat = down_weight[0]
    width = local.shape[1]
    wide = (width // 2) // 128 * 128
    wide_r = (width // 7 * 4) // 128 * 128
    hit = named == section
    chosen = jnp.any(hit, axis=1)
    slot = jnp.sum(jnp.where(hit, slot_index[0], 0), axis=1)
    weight = jnp.sum(jnp.where(hit, gate_scale[0], jnp.float32(0.0)), axis=1)
    route = jnp.where(chosen, slot + 1, 0).astype(jnp.int32)

    tok_prev = from_behind(local, "section", 1)
    cot_next = from_behind(grad_out, "section", -1)
    route_prev = from_behind(route, "section", 1)
    route_next = from_behind(route, "section", -1)

    places = jnp.arange(CAP, dtype=jnp.int32)
    mask = (places[:, None] == slot[None, :]) & chosen[None, :]
    table = mask.astype(jnp.bfloat16)
    sent = jnp.dot(table, local, preferred_element_type=jnp.float32).astype(jnp.bfloat16)
    cot_sent = jnp.dot(table, grad_out, preferred_element_type=jnp.float32).astype(jnp.bfloat16)
    wslot = jnp.sum(jnp.where(mask, weight[None, :], jnp.float32(0.0)), axis=1)
    carried = (weight[:, None] * grad_out.astype(jnp.float32)).astype(jnp.bfloat16)
    back = jnp.dot(table, carried, preferred_element_type=jnp.float32).astype(jnp.bfloat16)

    narrow = width - wide
    own_a, other_a = gather_wide(jnp.concatenate([sent[:, :wide], back[:, :wide]], axis=1))
    both_b = gather_narrow(jnp.concatenate([sent[:, wide:], back[:, wide:]], axis=1), first)
    zs = own_a.shape[0] // CAP

    def rows_in_order(rows, mat):
        mine = jnp.dot(rows[0], mat, preferred_element_type=jnp.float32).reshape(zs, CAP, -1)
        theirs = jnp.dot(rows[1], mat, preferred_element_type=jnp.float32).reshape(zs, CAP, -1)
        return in_order(first, mine, theirs, 1).reshape(zs * 2 * CAP, -1)

    sent_a = (own_a[:, :wide], other_a[:, :wide])
    back_a = (own_a[:, wide:], other_a[:, wide:])
    sent_b, back_b = both_b[:, :narrow], both_b[:, narrow:]

    f32 = jnp.float32
    gate = rows_in_order(sent_a, gate_mat[:wide]) + jnp.dot(
        sent_b, gate_mat[wide:], preferred_element_type=f32
    )
    up = rows_in_order(sent_a, up_mat[:wide]) + jnp.dot(
        sent_b, up_mat[wide:], preferred_element_type=f32
    )
    act, slope = silu_parts(gate)
    hidden = (act * up).astype(jnp.bfloat16)
    ahead_a = jnp.dot(hidden, down_mat[:, :wide_r], preferred_element_type=f32).astype(jnp.bfloat16)
    ahead_b = jnp.dot(hidden, down_mat[:, wide_r:], preferred_element_type=f32).astype(jnp.bfloat16)
    comb_b = scatter_narrow(ahead_b, first, CAP)
    grad_hidden = rows_in_order(back_a, down_mat[:, :wide].T) + jnp.dot(
        back_b, down_mat[:, wide:].T, preferred_element_type=f32
    )
    grad_up = (grad_hidden * act).astype(jnp.bfloat16)
    grad_gate = (grad_hidden * up * slope).astype(jnp.bfloat16)
    behind_b = (
        jnp.dot(grad_gate, gate_mat[wide_r:].T, preferred_element_type=f32)
        + jnp.dot(grad_up, up_mat[wide_r:].T, preferred_element_type=f32)
    ).astype(jnp.bfloat16)
    behind_a = (
        jnp.dot(grad_gate, gate_mat[:wide_r].T, preferred_element_type=f32)
        + jnp.dot(grad_up, up_mat[:wide_r].T, preferred_element_type=f32)
    ).astype(jnp.bfloat16)
    comb_a = scatter_wide(ahead_a, first, CAP)
    inw_b = scatter_narrow(behind_b, first, CAP)
    inw_a = scatter_wide(behind_a, first, CAP)
    combined = jnp.concatenate([comb_a, comb_b], axis=1)
    inward = jnp.concatenate([inw_a, inw_b], axis=1)

    out_rows = (sent.astype(f32) + wslot[:, None] * combined).astype(jnp.bfloat16)
    grad_rows = (cot_sent.astype(f32) + inward).astype(jnp.bfloat16)
    out_prev = from_behind(out_rows, "section", 1)
    grad_next = from_behind(grad_rows, "section", -1)
    next_input = pick_rows(route_prev, out_prev, tok_prev)
    prior_grad = pick_rows(route_next, grad_next, cot_next)
    return (next_input[None], prior_grad[None])


def solution(mesh):
    sections, experts = mesh.devices.shape
    grid = Mesh(mesh.devices.reshape(sections, 2, experts // 2), ("section", "xlo", "z"))
    ex = ("xlo", "z")
    in_specs = (
        P("section", ex, None),
        P("section", ex, None),
        P("section", ex, None),
        P("section", ex, None),
        P("section", ex, None),
        P("section", None, ex),
        P("section", None, ex),
        P("section", ex, None),
    )
    out_specs = (P("section", ex, None), P("section", ex, None))

    return jax.shard_map(body, mesh=grid, in_specs=in_specs, out_specs=out_specs, check_vma=False)
```

```python
import jax
import jax.numpy as jnp
from jax import lax
from jax.sharding import Mesh
from jax.sharding import PartitionSpec as P


CAP = 32
SWAP = [(0, 1), (1, 0)]


def from_behind(x, axis, by):
    length = lax.axis_size(axis)
    pairs = [(i, i + by) for i in range(length) if 0 <= i + by < length]
    return lax.ppermute(x, axis, pairs)


def silu_parts(gate):
    sig = jax.nn.sigmoid(gate)
    return (gate * sig, sig * (1.0 + gate * (1.0 - sig)))


def pick_rows(route, rows, bulk):
    places = jnp.arange(1, rows.shape[0] + 1, dtype=jnp.int32)
    table = (route[:, None] == places[None, :]).astype(rows.dtype)
    taken = jnp.dot(table, rows, preferred_element_type=jnp.float32).astype(rows.dtype)
    return jnp.where((route > 0)[:, None], taken, bulk)


def in_order(first, mine, other, axis):
    return jnp.where(first, jnp.stack([mine, other], axis), jnp.stack([other, mine], axis))


def gather_wide(x):
    own = lax.all_gather(x, "z", axis=0, tiled=True)
    other = lax.ppermute(own, "xlo", SWAP)
    return own, other


def gather_narrow(x, first):
    other = lax.ppermute(x, "xlo", SWAP)
    pair = in_order(first, x, other, 0).reshape(2 * x.shape[0], -1)
    return lax.all_gather(pair, "z", axis=0, tiled=True)


def scatter_wide(q, first, rows):
    zs = q.shape[0] // (2 * rows)
    q = q.reshape(zs, 2, rows, -1)
    keep = jnp.where(first, q[:, 0], q[:, 1])
    give = jnp.where(first, q[:, 1], q[:, 0])
    got = lax.ppermute(give, "xlo", SWAP)
    total = (keep.astype(jnp.float32) + got.astype(jnp.float32)).astype(jnp.bfloat16)
    part = lax.psum_scatter(total.reshape(zs * rows, -1), "z", scatter_dimension=0, tiled=True)
    return part.astype(jnp.float32)


def scatter_narrow(q, first, rows):
    t = lax.psum_scatter(q, "z", scatter_dimension=0, tiled=True)
    t = t.reshape(2, rows, -1)
    keep = jnp.where(first, t[0], t[1])
    give = jnp.where(first, t[1], t[0])
    got = lax.ppermute(give, "xlo", SWAP)
    return keep.astype(jnp.float32) + got.astype(jnp.float32)


def body(
    tokens, cotangent, expert_ids, slot_index, gate_scale, gate_weight, up_weight, down_weight
):
    section = lax.axis_index("section")
    first = lax.axis_index("xlo") == 0
    local = tokens[0]
    grad_out = cotangent[0]
    named = expert_ids[0]
    gate_mat = gate_weight[0]
    up_mat = up_weight[0]
    down_mat = down_weight[0]
    width = local.shape[1]
    wide = (width // 2) // 128 * 128
    wide_r = (width // 7 * 4) // 128 * 128
    hit = named == section
    chosen = jnp.any(hit, axis=1)
    slot = jnp.sum(jnp.where(hit, slot_index[0], 0), axis=1)
    weight = jnp.sum(jnp.where(hit, gate_scale[0], jnp.float32(0.0)), axis=1)
    route = jnp.where(chosen, slot + 1, 0).astype(jnp.int32)

    tok_prev = from_behind(local, "section", 1)
    cot_next = from_behind(grad_out, "section", -1)
    route_prev = from_behind(route, "section", 1)
    route_next = from_behind(route, "section", -1)

    places = jnp.arange(CAP, dtype=jnp.int32)
    mask = (places[:, None] == slot[None, :]) & chosen[None, :]
    table = mask.astype(jnp.bfloat16)
    sent = jnp.dot(table, local, preferred_element_type=jnp.float32).astype(jnp.bfloat16)
    cot_sent = jnp.dot(table, grad_out, preferred_element_type=jnp.float32).astype(jnp.bfloat16)
    wslot = jnp.sum(jnp.where(mask, weight[None, :], jnp.float32(0.0)), axis=1)
    carried = (weight[:, None] * grad_out.astype(jnp.float32)).astype(jnp.bfloat16)
    back = jnp.dot(table, carried, preferred_element_type=jnp.float32).astype(jnp.bfloat16)

    narrow = width - wide
    own_a, other_a = gather_wide(jnp.concatenate([sent[:, :wide], back[:, :wide]], axis=1))
    both_b = gather_narrow(jnp.concatenate([sent[:, wide:], back[:, wide:]], axis=1), first)
    zs = own_a.shape[0] // CAP

    def rows_in_order(rows, mat):
        mine = jnp.dot(rows[0], mat, preferred_element_type=jnp.float32)
        mine = mine.reshape(zs, CAP, -1)
        theirs = jnp.dot(rows[1], mat, preferred_element_type=jnp.float32).reshape(zs, CAP, -1)
        return in_order(first, mine, theirs, 1).reshape(zs * 2 * CAP, -1)

    sent_a = (own_a[:, :wide], other_a[:, :wide])
    back_a = (own_a[:, wide:], other_a[:, wide:])
    sent_b, back_b = both_b[:, :narrow], both_b[:, narrow:]

    f32 = jnp.float32
    gate = rows_in_order(sent_a, gate_mat[:wide]) + jnp.dot(
        sent_b, gate_mat[wide:], preferred_element_type=f32
    )
    up = rows_in_order(sent_a, up_mat[:wide]) + jnp.dot(
        sent_b, up_mat[wide:], preferred_element_type=f32
    )
    act, slope = silu_parts(gate)
    hidden = (act * up).astype(jnp.bfloat16)
    ahead_a = jnp.dot(hidden, down_mat[:, :wide_r], preferred_element_type=f32).astype(jnp.bfloat16)
    ahead_b = jnp.dot(hidden, down_mat[:, wide_r:], preferred_element_type=f32).astype(jnp.bfloat16)
    comb_b = scatter_narrow(ahead_b, first, CAP)
    grad_hidden = rows_in_order(back_a, down_mat[:, :wide].T) + jnp.dot(
        back_b, down_mat[:, wide:].T, preferred_element_type=f32
    )
    grad_up = (grad_hidden * act).astype(jnp.bfloat16)
    grad_gate = (grad_hidden * up * slope).astype(jnp.bfloat16)
    behind_b = (
        jnp.dot(grad_gate, gate_mat[wide_r:].T, preferred_element_type=f32)
        + jnp.dot(grad_up, up_mat[wide_r:].T, preferred_element_type=f32)
    ).astype(jnp.bfloat16)
    behind_a = (
        jnp.dot(grad_gate, gate_mat[:wide_r].T, preferred_element_type=f32)
        + jnp.dot(grad_up, up_mat[:wide_r].T, preferred_element_type=f32)
    ).astype(jnp.bfloat16)
    comb_a = scatter_wide(ahead_a, first, CAP)
    inw_b = scatter_narrow(behind_b, first, CAP)
    inw_a = scatter_wide(behind_a, first, CAP)
    combined = jnp.concatenate([comb_a, comb_b], axis=1)

    out_rows = (sent.astype(f32) + wslot[:, None] * combined).astype(jnp.bfloat16)
    rows_a = (cot_sent[:, :wide_r].astype(f32) + inw_a).astype(jnp.bfloat16)
    rows_b = (cot_sent[:, wide_r:].astype(f32) + inw_b).astype(jnp.bfloat16)
    out_prev = from_behind(out_rows, "section", 1)
    grad_next_b = from_behind(rows_b, "section", -1)
    grad_next_a = from_behind(rows_a, "section", -1)
    grad_next = jnp.concatenate([grad_next_a, grad_next_b], axis=1)
    next_input = pick_rows(route_prev, out_prev, tok_prev)
    prior_grad = pick_rows(route_next, grad_next, cot_next)
    return (next_input[None], prior_grad[None])


def solution(mesh):
    sections, experts = mesh.devices.shape
    grid = Mesh(mesh.devices.reshape(sections, 2, experts // 2), ("section", "xlo", "z"))
    ex = ("xlo", "z")
    in_specs = (
        P("section", ex, None),
        P("section", ex, None),
        P("section", ex, None),
        P("section", ex, None),
        P("section", ex, None),
        P("section", None, ex),
        P("section", None, ex),
        P("section", ex, None),
    )
    out_specs = (P("section", ex, None), P("section", ex, None))

    return jax.shard_map(body, mesh=grid, in_specs=in_specs, out_specs=out_specs, check_vma=False)
```
